256 devices in a mesh: dp: 8 (over x, z_hi), tensor: 32 (over y, z_lo, core).
Axes of the slice: x: 4, y: 4, z: 8 (z_hi: 2, z_lo: 4; z = z_hi * 4 + z_lo), core: 2. Of those that a mesh axis runs over, the one named last changes fastest.
Arguments:
- tokens: bfloat16 [8, 4096, 1280], P('dp', 'tensor'), may hold values from -6 to 6
- segment_ids: int32 [8, 4096], P('dp', 'tensor'), may hold values from 0 to 3, never falling along the last dimension, each value on 1 to 2048 neighbouring positions
- pack_of_group: int32 [32], replicated, may hold values from 0 to 31, each once
- w_qkv: bfloat16 [1280, 1920], replicated, may hold values from -0.11320094 to 0.11320094
- qk_gain: float32 [640], replicated, may hold values from 0.5 to 7
- w_out: bfloat16 [640, 1280], replicated, may hold values from -0.25 to 0.25
- alpha_attn: float32 [1280], replicated, may hold values from 0.05 to 0.6
- w_up: bfloat16 [1280, 5120], P(None, 'dp'), may hold values from -0.15625 to 0.15625
- w_gate: bfloat16 [1280, 5120], P(None, 'dp'), may hold values from -0.15625 to 0.15625
- up_gain: float32 [5120], P('dp'), may hold values from 0.5 to 2
- gate_gain: float32 [5120], P('dp'), may hold values from 0.5 to 2
- w_down: bfloat16 [5120, 1280], P('dp'), may hold values from -0.078125 to 0.078125
- alpha_mlp: float32 [1280], replicated, may hold values from 0.05 to 0.6
- w_vocab: bfloat16 [1280, 32000], P(None, ('dp', 'tensor')), may hold values from -0.15625 to 0.15625
- logit_gain: bfloat16 [32000], P(('dp', 'tensor')), may hold values from 1 to 10
Outputs:
- result_rows: bfloat16 [8, 4096, 1280], P('dp', 'tensor')
- request_norm: float32 [32], replicated
- max_logit: float32 [32], replicated
The draws below stay inside these ranges and needn't reach their ends.
Inputs may be any that keep to these rules, and one draw needn't show every extreme that they name: `segment_ids`: within a pack the request numbers never fall, every request 0 to 3 has one or more tokens, and one request has exactly 2048 tokens.
All inputs are finite; a program needn't handle non-finite values.
Results may differ from the reference program's by a relative error of at most 0.013.
Values may be sent and summed in bfloat16 or wider, within the bound.
No kernel may reach another device: no remote copies, remote signals or barrier semaphores. Data moves between devices by JAX's collectives and lax.ppermute only.
A program may use at most 128 MiB of HBM per device.

```python
import math
import jax
import jax.numpy as jnp
import numpy as np
from jax import lax

D = 1280
HEADS = 10
HD = 64
FF = 5120
VOCAB = 32000
REQS = 4
PACK = 4096
N_DP = 8


def draw_tokens(key, part):
    drawn = jnp.clip(jax.random.normal(jax.random.fold_in(key, 21), (N_DP, PACK, D), jnp.float32), -6.0, 6.0)
    return drawn.astype(jnp.bfloat16)


def draw_w_qkv(key, part):
    head_width = HEADS * HD
    drawn = jnp.clip(jax.random.normal(jax.random.fold_in(key, 11), (D, 3 * head_width), jnp.float32), -4.0, 4.0) * D ** (-0.5)
    return drawn.astype(jnp.bfloat16)


def draw_qk_gain(key, part):
    log_low = jnp.log(0.5)
    log_high = jnp.log(3.0)
    drawn = jnp.exp(jax.random.uniform(jax.random.fold_in(key, 13), (HEADS, HD), jnp.float32, log_low, log_high))
    return drawn.reshape(HEADS * HD)


def level_of(rng, shape, pieces, least, top_value):
    gain = 1.0
    for dim, blocks in pieces:
        draws = jax.random.uniform(jax.random.fold_in(jax.random.fold_in(rng, 6), dim), (blocks,), jnp.float32, least / len(pieces), top_value / len(pieces))
        gain = gain * jnp.repeat(jnp.exp(draws), shape[dim] // blocks).reshape((-1,) + (1,) * (len(shape) - 1 - dim))
    return gain


def length_profile(count, total, most, skew):
    portions = [(1 << 20) // math.isqrt(grade ** skew) + 1 for grade in range(2, count + 1)]
    rest, given = total - most - (count - 1), [1] * (count - 1)
    while rest > 0:
        free = [i for i in range(count - 1) if given[i] < most]
        pool, left = sum([portions[i] for i in free]), rest
        for i in free:
            extra = min(most - given[i], max(1, left * portions[i] // pool), rest)
            given[i] = given[i] + extra
            rest = rest - extra
    return np.array([most] + given)


def uneven_parts(own_key, amount, total, reach, lean):
    if amount == 2:
        one = jax.random.randint(own_key, (), max(1, total - reach), min(reach, total - 1) + 1)
        return jnp.stack([one, total - one])
    lengths = jnp.asarray(length_profile(amount, total, reach, lean), jnp.int32)
    couples = (amount - 1) // 2
    giver, sink = lengths[1:1 + 2 * couples:2], lengths[2:2 + 2 * couples:2]
    margin = jnp.minimum(giver - 1, reach - sink)
    moved = jax.random.randint(jax.random.fold_in(own_key, 1), (couples,), 0, 1 << 20) % (margin + 1)
    lengths = lengths.at[1:1 + 2 * couples:2].set(giver - moved).at[2:2 + 2 * couples:2].set(sink + moved)
    return lengths[jax.random.permutation(jax.random.fold_in(own_key, 2), amount)]


def noise(key, shape, width, bound, shards=(), kind=jnp.bfloat16):
    factor_of = level_of(key, shape, shards, -0.22, 0.18) if shards else 1.0
    array = jax.random.normal(key, shape, jnp.float32) * width * factor_of
    return jnp.minimum(jnp.maximum(array, -bound), bound).astype(kind)


def setup_inputs(seed: int = 0) -> dict:
    key_list = jax.random.split(jax.random.key(seed), 16)
    tokens = draw_tokens(jax.random.fold_in(key_list[15], 71), 0)
    segment_ids = jax.vmap(lambda own: jnp.searchsorted(jnp.cumsum(uneven_parts(own, REQS, PACK, PACK // 2, 2)), jnp.arange(PACK), side="right"))(jax.random.split(key_list[1], N_DP)).reshape((N_DP, PACK)).astype(jnp.int32)
    pack_of_group = jax.random.permutation(key_list[2], N_DP * REQS).astype(jnp.int32)
    w_qkv = draw_w_qkv(jax.random.fold_in(key_list[15], 71), 0)
    qk_gain = draw_qk_gain(jax.random.fold_in(key_list[15], 71), 0)
    w_out = noise(key_list[5], (HEADS * HD, D), (HEADS * HD) ** -0.5, 0.25)
    alpha_attn = jnp.clip(jnp.exp(jax.random.uniform(key_list[6], (D,), jnp.float32, math.log(0.05), math.log(0.6))), 0.05, 0.6)
    w_up = noise(key_list[7], (D, FF), D ** -0.5, 0.15625, ((1, 8),))
    w_gate = noise(key_list[8], (D, FF), D ** -0.5, 0.15625, ((1, 8),))
    up_gain = jnp.clip(jnp.exp(math.log(2.0) - 1.3862944 * jax.random.uniform(key_list[9], (FF,), jnp.float32) ** level_of(key_list[9], (FF,), ((0, 8),), -0.2, 0.2)), 0.5, 2.0)
    gate_gain = jnp.clip(jnp.exp(math.log(2.0) - 1.3862944 * jax.random.uniform(key_list[10], (FF,), jnp.float32) ** level_of(key_list[10], (FF,), ((0, 8),), -0.2, 0.2)), 0.5, 2.0)
    w_down = noise(key_list[11], (FF, D), FF ** -0.5, 0.078125, ((0, 8),))
    alpha_mlp = jnp.clip(jnp.exp(jax.random.uniform(key_list[12], (D,), jnp.float32, math.log(0.05), math.log(0.6))), 0.05, 0.6)
    w_vocab = noise(key_list[13], (D, VOCAB), D ** -0.5, 0.15625, ((1, 256),))
    logit_gain = jnp.clip(jnp.exp(math.log(10.0) - 2.3025851 * jax.random.uniform(key_list[14], (VOCAB,), jnp.float32) ** level_of(key_list[14], (VOCAB,), ((0, 256),), -0.2, 0.2)), 1.0, 10.0).astype(jnp.bfloat16)
    return {"tokens": tokens, "segment_ids": segment_ids, "pack_of_group": pack_of_group, "w_qkv": w_qkv, "qk_gain": qk_gain, "w_out": w_out, "alpha_attn": alpha_attn, "w_up": w_up, "w_gate": w_gate, "up_gain": up_gain, "gate_gain": gate_gain, "w_down": w_down, "alpha_mlp": alpha_mlp, "w_vocab": w_vocab, "logit_gain": logit_gain}


EPSILON = 1e-06
NEGATIVE = -1e+30

def normalize(values):
    return values * lax.rsqrt(lax.optimization_barrier(jnp.mean(values * values, axis=-1, keepdims=True)) + EPSILON)

def head_norm(values, qk_gain):
    reshaped = values.reshape(values.shape[0], HEADS, HD)
    return (normalize(reshaped) * qk_gain.reshape(HEADS, HD)).astype(jnp.bfloat16)

def reference(tokens, segment_ids, pack_of_group, w_qkv, qk_gain, w_out, alpha_attn, w_up, w_gate, up_gain, gate_gain, w_down, alpha_mlp, w_vocab, logit_gain):
    head_width = HEADS * HD
    query_block = math.gcd(PACK, 512)
    width_dev = FF // N_DP

    def one_group(operands):
        group_rows, segments = operands
        start_rows = normalize(group_rows.astype(jnp.float32)).astype(jnp.bfloat16)
        projected = jnp.dot(start_rows, w_qkv, preferred_element_type=jnp.float32)
        queries = head_norm(projected[:, :head_width], qk_gain)
        keys_f32 = head_norm(projected[:, head_width:2 * head_width], qk_gain).astype(jnp.float32)
        values_f32 = projected[:, 2 * head_width:].astype(jnp.bfloat16).astype(jnp.float32).reshape(PACK, HEADS, HD)
        positions = jnp.arange(PACK, dtype=jnp.int32)

        def attend(block_index):
            offset = (block_index * query_block).astype(jnp.int32)
            query_rows = lax.dynamic_slice_in_dim(queries, offset, query_block, 0).astype(jnp.float32)
            query_segs = lax.dynamic_slice_in_dim(segments, offset, query_block, 0)
            query_pos = offset + jnp.arange(query_block, dtype=jnp.int32)
            scores = jnp.einsum('qhd,khd->hqk', query_rows, keys_f32) / math.sqrt(HD)
            allowed = (segments[None, :] == query_segs[:, None]) & (positions[None, :] <= query_pos[:, None])
            row_max = lax.optimization_barrier(jnp.max(jnp.where(allowed[None], scores, NEGATIVE), axis=2, keepdims=True))
            weights = jnp.where(allowed[None], jnp.exp(scores - row_max), 0.0)
            weight_sum = lax.optimization_barrier(jnp.sum(weights, axis=2))
            rounded = lax.optimization_barrier(weights.astype(jnp.bfloat16)).astype(jnp.float32)
            attended = jnp.einsum('hqk,khd->qhd', rounded, values_f32) / weight_sum.T[:, :, None]
            return attended.reshape(query_block, head_width).astype(jnp.bfloat16)
        attended = lax.map(attend, jnp.arange(PACK // query_block, dtype=jnp.int32)).reshape(PACK, head_width)
        attn_rows = normalize(jnp.dot(attended, w_out, preferred_element_type=jnp.float32))
        residual_in = start_rows.astype(jnp.float32)
        mid_rows = normalize(residual_in + alpha_attn * (attn_rows - residual_in)).astype(jnp.bfloat16)
        up_proj = jnp.dot(mid_rows, w_up, preferred_element_type=jnp.float32) * up_gain
        gate_proj = jnp.dot(mid_rows, w_gate, preferred_element_type=jnp.float32) * gate_gain
        hidden = (up_proj * jax.nn.silu(gate_proj)).astype(jnp.bfloat16)
        hidden_blocks = hidden.reshape(PACK, N_DP, width_dev).transpose(1, 0, 2)
        down_blocks = w_down.reshape(N_DP, width_dev, D)

        def add_block(mixed_sum, pair):
            part = jnp.dot(pair[0], pair[1], preferred_element_type=jnp.float32)
            part = lax.optimization_barrier(part.astype(jnp.bfloat16)).astype(jnp.float32)
            return (mixed_sum + part, None)
        mixed_sum, _ = lax.scan(add_block, jnp.zeros((PACK, D), jnp.float32), (hidden_blocks, down_blocks))
        mlp_rows = normalize(mixed_sum)
        residual_mid = mid_rows.astype(jnp.float32)
        result_rows = normalize(residual_mid + alpha_mlp * (mlp_rows - residual_mid)).astype(jnp.bfloat16)
        member = (segments[:, None] == jnp.arange(REQS, dtype=jnp.int32)[None, :]).astype(jnp.float32)
        following = jnp.concatenate([segments[1:], jnp.full((1,), -1, jnp.int32)])
        chosen = member * (following != segments)[:, None].astype(jnp.float32)
        result_f32 = result_rows.astype(jnp.float32)
        row_sums = jnp.dot(member.T, result_f32, precision=lax.Precision.HIGHEST)
        last_rows = jnp.dot(chosen.T, result_f32, precision=lax.Precision.HIGHEST)
        counts = lax.optimization_barrier(jnp.sum(member, axis=0))
        request_mean = row_sums / counts[:, None]
        group_norm = jnp.sqrt(lax.optimization_barrier(jnp.mean(request_mean * request_mean, axis=1)))
        return (result_rows, group_norm, last_rows)
    result_rows, group_norm, last_rows = lax.map(one_group, (tokens, segment_ids))
    every_last = last_rows.reshape(N_DP * REQS, D).astype(jnp.bfloat16)
    logits = jnp.dot(every_last, w_vocab, preferred_element_type=jnp.float32) * logit_gain.astype(jnp.float32)
    group_max = lax.optimization_barrier(jnp.max(logits, axis=1))
    request_norm = jnp.zeros((N_DP * REQS,), jnp.float32).at[pack_of_group].set(group_norm.reshape(N_DP * REQS))
    max_logit = jnp.zeros((N_DP * REQS,), jnp.float32).at[pack_of_group].set(group_max)
    return (result_rows, request_norm, max_logit)
```

```python
import math

import jax
import jax.numpy as jnp
from jax import lax
from jax.sharding import PartitionSpec as P

HEADS = 10
HD = 64
REQS = 4


EPSILON = 1e-06
NEGATIVE = -1e30


def normalize(values):
    return values * lax.rsqrt(jnp.mean(values * values, axis=-1, keepdims=True) + EPSILON)


def head_norm(values, qk_gain):
    reshaped = values.reshape(values.shape[0], HEADS, HD)
    return (normalize(reshaped) * qk_gain.reshape(HEADS, HD)).astype(jnp.bfloat16)


def local(
    tokens,
    segment_ids,
    pack_of_group,
    w_qkv,
    qk_gain,
    w_out,
    alpha_attn,
    w_up,
    w_gate,
    up_gain,
    gate_gain,
    w_down,
    alpha_mlp,
    w_vocab,
    logit_gain,
):
    row_count = tokens.shape[1]
    head_width = HEADS * HD
    segments = segment_ids[0]
    tensor_index = lax.axis_index("tensor")
    positions = tensor_index * row_count + jnp.arange(row_count, dtype=jnp.int32)
    request_numbers = jnp.arange(REQS, dtype=jnp.int32)
    start_rows = normalize(tokens[0].astype(jnp.float32)).astype(jnp.bfloat16)
    projected = jnp.dot(start_rows, w_qkv, preferred_element_type=jnp.float32)
    queries = head_norm(projected[:, :head_width], qk_gain)
    key_rows = head_norm(projected[:, head_width : 2 * head_width], qk_gain).reshape(
        row_count, head_width
    )
    value_rows = projected[:, 2 * head_width :].astype(jnp.bfloat16)
    score_scale = 1.0 / math.sqrt(HD)
    offset = jnp.int32(0)
    state_now = (
        jnp.full((HEADS, row_count), NEGATIVE, jnp.float32),
        jnp.zeros((HEADS, row_count), jnp.float32),
        jnp.zeros((HEADS, row_count, HD), jnp.float32),
    )
    seg_block = jnp.zeros((8, 2 * head_width), jnp.bfloat16).at[0, :row_count].set(
        segments.astype(jnp.bfloat16)
    )
    packed = jnp.concatenate(
        [jnp.concatenate([key_rows, value_rows], axis=1), seg_block], axis=0
    )
    gathered = lax.all_gather(packed, "tensor", axis=0, tiled=False)
    key_all = gathered[:, :row_count, :head_width].reshape(-1, head_width)
    value_all = gathered[:, :row_count, head_width:].reshape(-1, head_width)
    seg_all = gathered[:, row_count, :row_count].reshape(-1).astype(jnp.int32)
    tally = jnp.sum((seg_all[:, None] == request_numbers[None, :]).astype(jnp.int32), axis=0)
    total_keys = key_all.shape[0]
    step_size = math.gcd(total_keys, 512)
    for begin in range(0, total_keys, step_size):
        key_part = key_all[begin : begin + step_size]
        value_part = value_all[begin : begin + step_size]
        seg_part = seg_all[begin : begin + step_size]
        key_pos = offset + begin + jnp.arange(step_size, dtype=jnp.int32)
        update_running_max, update_weight_sum, update_weighted = state_now
        key_count = key_part.shape[0]
        key_heads = key_part.reshape(key_count, HEADS, HD)
        value_heads = value_part.reshape(key_count, HEADS, HD)
        scores = (
            jnp.einsum("qhd,khd->hqk", queries, key_heads, preferred_element_type=jnp.float32)
            * score_scale
        )
        allowed = (seg_part[None, :] == segments[:, None]) & (
            key_pos[None, :] <= positions[:, None]
        )
        new_max = jnp.maximum(
            update_running_max, jnp.max(jnp.where(allowed[None], scores, NEGATIVE), axis=2)
        )
        weights = jnp.where(allowed[None], jnp.exp(scores - new_max[:, :, None]), 0.0)
        factor = jnp.exp(update_running_max - new_max)
        update_weight_sum = update_weight_sum * factor + jnp.sum(weights, axis=2)
        update_weighted = update_weighted * factor[:, :, None] + jnp.einsum(
            "hqk,khd->hqd",
            weights.astype(jnp.bfloat16),
            value_heads,
            preferred_element_type=jnp.float32,
        )
        state_now = (new_max, update_weight_sum, update_weighted)
    folded, tally = (state_now, tally)
    running_max, weight_sum, weighted = folded
    attended = (
        (weighted / weight_sum[:, :, None])
        .transpose(1, 0, 2)
        .reshape(row_count, head_width)
        .astype(jnp.bfloat16)
    )
    attn_rows = normalize(jnp.dot(attended, w_out, preferred_element_type=jnp.float32))
    residual_in = start_rows.astype(jnp.float32)
    mid_rows = normalize(residual_in + alpha_attn * (attn_rows - residual_in)).astype(jnp.bfloat16)
    received = lax.all_gather(mid_rows, "dp", axis=0, tiled=True)
    up_proj = jnp.dot(received, w_up, preferred_element_type=jnp.float32) * up_gain
    gate_proj = jnp.dot(received, w_gate, preferred_element_type=jnp.float32) * gate_gain
    hidden = (up_proj * jax.nn.silu(gate_proj)).astype(jnp.bfloat16)
    mixed_sum = lax.psum_scatter(
        jnp.dot(hidden, w_down, preferred_element_type=jnp.float32).astype(jnp.bfloat16),
        "dp",
        scatter_dimension=0,
        tiled=True,
    ).astype(jnp.float32)
    mlp_rows = normalize(mixed_sum)
    residual_mid = mid_rows.astype(jnp.float32)
    result_rows = normalize(residual_mid + alpha_mlp * (mlp_rows - residual_mid)).astype(
        jnp.bfloat16
    )
    request_ends = jnp.cumsum(tally) - 1
    same_request = segments[:, None] == request_numbers[None, :]
    row_end = jnp.sum(jnp.where(same_request, request_ends[None, :], 0), axis=1)
    is_last = positions == row_end
    member = same_request.astype(jnp.float32)
    chosen = member * is_last[:, None].astype(jnp.float32)
    result_f32 = result_rows.astype(jnp.float32)
    row_sums = jnp.dot(member.T, result_f32, precision=lax.Precision.HIGHEST)
    last_rows = jnp.dot(chosen.T, result_f32, precision=lax.Precision.HIGHEST)
    partial = jnp.concatenate([row_sums, last_rows], axis=0)
    summed = jnp.sum(lax.all_gather(partial, "tensor", axis=0, tiled=False), axis=0)
    row_sums, last_rows = summed[:REQS], summed[REQS:]
    counts = tally.astype(jnp.float32)
    request_mean = row_sums / counts[:, None]
    group_norm = jnp.sqrt(jnp.mean(request_mean * request_mean, axis=1))
    slot_count = lax.axis_size("dp") * REQS
    norm_row = jnp.zeros((1, last_rows.shape[1]), jnp.float32).at[0, :REQS].set(group_norm)
    pack_stats = lax.all_gather(
        jnp.concatenate([last_rows, norm_row], axis=0), "dp", axis=0, tiled=False
    )
    every_last = pack_stats[:, :REQS].reshape(slot_count, -1)
    every_norm = pack_stats[:, REQS, :REQS].reshape(slot_count)
    logits = jnp.dot(
        every_last.astype(jnp.bfloat16), w_vocab, preferred_element_type=jnp.float32
    ) * logit_gain.astype(jnp.float32)
    every_max = lax.pmax(jnp.max(logits, axis=1), ("dp", "tensor"))
    placement = (pack_of_group[:, None] == jnp.arange(slot_count, dtype=jnp.int32)[None, :]).astype(
        jnp.float32
    )
    request_norm = jnp.dot(every_norm, placement, precision=lax.Precision.HIGHEST)
    max_logit = jnp.dot(every_max, placement, precision=lax.Precision.HIGHEST)
    return (result_rows[None], request_norm, max_logit)


def solution(mesh):
    return jax.shard_map(
        local,
        mesh=mesh,
        in_specs=(
            P("dp", "tensor", None),
            P("dp", "tensor"),
            P(),
            P(),
            P(),
            P(),
            P(),
            P(None, "dp"),
            P(None, "dp"),
            P("dp"),
            P("dp"),
            P("dp", None),
            P(),
            P(None, ("dp", "tensor")),
            P(("dp", "tensor")),
        ),
        out_specs=(P("dp", "tensor", None), P(), P()),
        check_vma=False,
    )
```

```python
import math

import jax
import jax.numpy as jnp
from jax import lax
from jax.sharding import PartitionSpec as P

HEADS = 10
HD = 64
REQS = 4


EPSILON = 1e-06
NEGATIVE = -1e30


def normalize(values):
    return values * lax.rsqrt(jnp.mean(values * values, axis=-1, keepdims=True) + EPSILON)


def head_norm(values, qk_gain):
    reshaped = values.reshape(values.shape[0], HEADS, HD)
    return (normalize(reshaped) * qk_gain.reshape(HEADS, HD)).astype(jnp.bfloat16)


def local(
    tokens,
    segment_ids,
    pack_of_group,
    w_qkv,
    qk_gain,
    w_out,
    alpha_attn,
    w_up,
    w_gate,
    up_gain,
    gate_gain,
    w_down,
    alpha_mlp,
    w_vocab,
    logit_gain,
):
    row_count = tokens.shape[1]
    head_width = HEADS * HD
    segments = segment_ids[0]
    tensor_index = lax.axis_index("tensor")
    positions = tensor_index * row_count + jnp.arange(row_count, dtype=jnp.int32)
    request_numbers = jnp.arange(REQS, dtype=jnp.int32)
    start_rows = normalize(tokens[0].astype(jnp.float32)).astype(jnp.bfloat16)
    projected = jnp.dot(start_rows, w_qkv, preferred_element_type=jnp.float32)
    queries = head_norm(projected[:, :head_width], qk_gain)
    key_rows = head_norm(projected[:, head_width : 2 * head_width], qk_gain).reshape(
        row_count, head_width
    )
    value_rows = projected[:, 2 * head_width :].astype(jnp.bfloat16)
    score_scale = 1.0 / math.sqrt(HD)
    seg_block = jnp.zeros((8, 2 * head_width), jnp.bfloat16).at[0, :row_count].set(
        segments.astype(jnp.bfloat16)
    )
    packed = jnp.concatenate(
        [jnp.concatenate([key_rows, value_rows], axis=1), seg_block], axis=0
    )
    gathered = lax.all_gather(packed, "tensor", axis=0, tiled=False)
    key_all = gathered[:, :row_count, :head_width].reshape(-1, head_width)
    value_all = gathered[:, :row_count, head_width:].reshape(-1, head_width)
    seg_all = gathered[:, row_count, :row_count].reshape(-1).astype(jnp.int32)
    tally = jnp.sum((seg_all[:, None] == request_numbers[None, :]).astype(jnp.int32), axis=0)
    total_keys = key_all.shape[0]
    key_pos = jnp.arange(total_keys, dtype=jnp.int32)
    key_heads = key_all.reshape(total_keys, HEADS, HD)
    value_heads = value_all.reshape(total_keys, HEADS, HD)
    scores = (
        jnp.einsum("qhd,khd->hqk", queries, key_heads, preferred_element_type=jnp.float32)
        * score_scale
    )
    allowed = (seg_all[None, :] == segments[:, None]) & (key_pos[None, :] <= positions[:, None])
    row_max = jnp.max(jnp.where(allowed[None], scores, NEGATIVE), axis=2)
    weights = jnp.where(allowed[None], jnp.exp(scores - row_max[:, :, None]), 0.0)
    weight_sum = jnp.sum(weights, axis=2)
    weighted = jnp.einsum(
        "hqk,khd->hqd",
        weights.astype(jnp.bfloat16),
        value_heads,
        preferred_element_type=jnp.float32,
    )
    attended = (
        (weighted / weight_sum[:, :, None])
        .transpose(1, 0, 2)
        .reshape(row_count, head_width)
        .astype(jnp.bfloat16)
    )
    attn_rows = normalize(jnp.dot(attended, w_out, preferred_element_type=jnp.float32))
    residual_in = start_rows.astype(jnp.float32)
    mid_rows = normalize(residual_in + alpha_attn * (attn_rows - residual_in)).astype(jnp.bfloat16)
    received = lax.all_gather(mid_rows, "dp", axis=0, tiled=True)
    up_proj = jnp.dot(received, w_up, preferred_element_type=jnp.float32) * up_gain
    gate_proj = jnp.dot(received, w_gate, preferred_element_type=jnp.float32) * gate_gain
    hidden = (up_proj * jax.nn.silu(gate_proj)).astype(jnp.bfloat16)
    mixed_sum = lax.psum_scatter(
        jnp.dot(hidden, w_down, preferred_element_type=jnp.float32).astype(jnp.bfloat16),
        "dp",
        scatter_dimension=0,
        tiled=True,
    ).astype(jnp.float32)
    mlp_rows = normalize(mixed_sum)
    residual_mid = mid_rows.astype(jnp.float32)
    result_rows = normalize(residual_mid + alpha_mlp * (mlp_rows - residual_mid)).astype(
        jnp.bfloat16
    )
    request_ends = jnp.cumsum(tally) - 1
    same_request = segments[:, None] == request_numbers[None, :]
    row_end = jnp.sum(jnp.where(same_request, request_ends[None, :], 0), axis=1)
    is_last = positions == row_end
    member = same_request.astype(jnp.float32)
    chosen = member * is_last[:, None].astype(jnp.float32)
    result_f32 = result_rows.astype(jnp.float32)
    row_sums = jnp.dot(member.T, result_f32, precision=lax.Precision.HIGHEST)
    last_rows = jnp.dot(chosen.T, result_f32, precision=lax.Precision.HIGHEST)
    partial = jnp.concatenate([row_sums, last_rows], axis=0)
    summed = jnp.sum(lax.all_gather(partial, "tensor", axis=0, tiled=False), axis=0)
    row_sums, last_rows = summed[:REQS], summed[REQS:]
    counts = tally.astype(jnp.float32)
    request_mean = row_sums / counts[:, None]
    group_norm = jnp.sqrt(jnp.mean(request_mean * request_mean, axis=1))
    slot_count = lax.axis_size("dp") * REQS
    norm_row = jnp.zeros((1, last_rows.shape[1]), jnp.float32).at[0, :REQS].set(group_norm)
    pack_stats = lax.all_gather(
        jnp.concatenate([last_rows, norm_row], axis=0), "dp", axis=0, tiled=False
    )
    every_last = pack_stats[:, :REQS].reshape(slot_count, -1)
    every_norm = pack_stats[:, REQS, :REQS].reshape(slot_count)
    logits = jnp.dot(
        every_last.astype(jnp.bfloat16), w_vocab, preferred_element_type=jnp.float32
    ) * logit_gain.astype(jnp.float32)
    every_max = lax.pmax(jnp.max(logits, axis=1), ("dp", "tensor"))
    placement = (pack_of_group[:, None] == jnp.arange(slot_count, dtype=jnp.int32)[None, :]).astype(
        jnp.float32
    )
    request_norm = jnp.dot(every_norm, placement, precision=lax.Precision.HIGHEST)
    max_logit = jnp.dot(every_max, placement, precision=lax.Precision.HIGHEST)
    return (result_rows[None], request_norm, max_logit)


def solution(mesh):
    return jax.shard_map(
        local,
        mesh=mesh,
        in_specs=(
            P("dp", "tensor", None),
            P("dp", "tensor"),
            P(),
            P(),
            P(),
            P(),
            P(),
            P(None, "dp"),
            P(None, "dp"),
            P("dp"),
            P("dp"),
            P("dp", None),
            P(),
            P(None, ("dp", "tensor")),
            P(("dp", "tensor")),
        ),
        out_specs=(P("dp", "tensor", None), P(), P()),
        check_vma=False,
    )
```

```python
import math

import jax
import jax.numpy as jnp
from jax import lax
from jax.sharding import PartitionSpec as P

HEADS = 10
HD = 64
REQS = 4


EPSILON = 1e-06
NEGATIVE = -1e30


def normalize(values):
    return values * lax.rsqrt(jnp.mean(values * values, axis=-1, keepdims=True) + EPSILON)


def head_norm(values, qk_gain):
    reshaped = values.reshape(values.shape[0], HEADS, HD)
    return (normalize(reshaped) * qk_gain.reshape(HEADS, HD)).astype(jnp.bfloat16)


def local(
    tokens,
    segment_ids,
    pack_of_group,
    w_qkv,
    qk_gain,
    w_out,
    alpha_attn,
    w_up,
    w_gate,
    up_gain,
    gate_gain,
    w_down,
    alpha_mlp,
    w_vocab,
    logit_gain,
):
    row_count = tokens.shape[1]
    head_width = HEADS * HD
    segments = segment_ids[0]
    tensor_index = lax.axis_index("tensor")
    positions = tensor_index * row_count + jnp.arange(row_count, dtype=jnp.int32)
    request_numbers = jnp.arange(REQS, dtype=jnp.int32)
    start_rows = normalize(tokens[0].astype(jnp.float32)).astype(jnp.bfloat16)
    projected = jnp.dot(start_rows, w_qkv, preferred_element_type=jnp.float32)
    queries = head_norm(projected[:, :head_width], qk_gain)
    key_rows = head_norm(projected[:, head_width : 2 * head_width], qk_gain).reshape(
        row_count, head_width
    )
    value_rows = projected[:, 2 * head_width :].astype(jnp.bfloat16)
    score_scale = 1.0 / math.sqrt(HD)
    seg_block = jnp.zeros((8, 2 * head_width), jnp.bfloat16).at[0, :row_count].set(
        segments.astype(jnp.bfloat16)
    )
    packed = jnp.concatenate(
        [jnp.concatenate([key_rows, value_rows], axis=1), seg_block], axis=0
    )
    gathered = lax.all_gather(packed, "tensor", axis=0, tiled=False)
    key_all = gathered[:, :row_count, :head_width].reshape(-1, head_width)
    value_all = gathered[:, :row_count, head_width:].reshape(-1, head_width)
    seg_all = gathered[:, row_count, :row_count].reshape(-1).astype(jnp.int32)
    tally = jnp.sum((seg_all[:, None] == request_numbers[None, :]).astype(jnp.int32), axis=0)
    total_keys = key_all.shape[0]
    key_pos = jnp.arange(total_keys, dtype=jnp.int32)
    head_of_column = jnp.arange(head_width, dtype=jnp.int32) // HD
    head_mask = (jnp.arange(HEADS, dtype=jnp.int32)[:, None] == head_of_column[None, :]).astype(
        jnp.bfloat16
    )
    query_flat = queries.reshape(row_count, head_width)
    query_blocks = (query_flat[None, :, :] * head_mask[:, None, :]).reshape(
        HEADS * row_count, head_width
    )
    scores = (
        lax.dot_general(
            query_blocks,
            key_all,
            (((1,), (1,)), ((), ())),
            preferred_element_type=jnp.float32,
        ).reshape(HEADS, row_count, total_keys)
        * score_scale
    )
    allowed = (seg_all[None, :] == segments[:, None]) & (key_pos[None, :] <= positions[:, None])
    row_max = jnp.max(jnp.where(allowed[None], scores, NEGATIVE), axis=2)
    weights = jnp.where(allowed[None], jnp.exp(scores - row_max[:, :, None]), 0.0)
    weight_sum = jnp.sum(weights, axis=2)
    weighted = jnp.dot(
        weights.astype(jnp.bfloat16).reshape(HEADS * row_count, total_keys),
        value_all,
        preferred_element_type=jnp.float32,
    ).reshape(HEADS, row_count, head_width)
    attended = jnp.sum(
        (weighted / weight_sum[:, :, None]) * head_mask[:, None, :].astype(jnp.float32), axis=0
    ).astype(jnp.bfloat16)
    attn_rows = normalize(jnp.dot(attended, w_out, preferred_element_type=jnp.float32))
    residual_in = start_rows.astype(jnp.float32)
    mid_rows = normalize(residual_in + alpha_attn * (attn_rows - residual_in)).astype(jnp.bfloat16)
    received = lax.all_gather(mid_rows, "dp", axis=0, tiled=True)
    up_proj = jnp.dot(received, w_up, preferred_element_type=jnp.float32) * up_gain
    gate_proj = jnp.dot(received, w_gate, preferred_element_type=jnp.float32) * gate_gain
    hidden = (up_proj * jax.nn.silu(gate_proj)).astype(jnp.bfloat16)
    mixed_sum = lax.psum_scatter(
        jnp.dot(hidden, w_down, preferred_element_type=jnp.float32).astype(jnp.bfloat16),
        "dp",
        scatter_dimension=0,
        tiled=True,
    ).astype(jnp.float32)
    mlp_rows = normalize(mixed_sum)
    residual_mid = mid_rows.astype(jnp.float32)
    result_rows = normalize(residual_mid + alpha_mlp * (mlp_rows - residual_mid)).astype(
        jnp.bfloat16
    )
    request_ends = jnp.cumsum(tally) - 1
    same_request = segments[:, None] == request_numbers[None, :]
    row_end = jnp.sum(jnp.where(same_request, request_ends[None, :], 0), axis=1)
    is_last = positions == row_end
    member = same_request.astype(jnp.float32)
    chosen = member * is_last[:, None].astype(jnp.float32)
    result_f32 = result_rows.astype(jnp.float32)
    row_sums = jnp.dot(member.T, result_f32, precision=lax.Precision.HIGHEST)
    last_rows = jnp.dot(chosen.T, result_f32, precision=lax.Precision.HIGHEST)
    partial = jnp.concatenate([row_sums, last_rows], axis=0)
    summed = jnp.sum(lax.all_gather(partial, "tensor", axis=0, tiled=False), axis=0)
    row_sums, last_rows = summed[:REQS], summed[REQS:]
    counts = tally.astype(jnp.float32)
    request_mean = row_sums / counts[:, None]
    group_norm = jnp.sqrt(jnp.mean(request_mean * request_mean, axis=1))
    slot_count = lax.axis_size("dp") * REQS
    norm_row = jnp.zeros((1, last_rows.shape[1]), jnp.float32).at[0, :REQS].set(group_norm)
    pack_stats = lax.all_gather(
        jnp.concatenate([last_rows, norm_row], axis=0), "dp", axis=0, tiled=False
    )
    every_last = pack_stats[:, :REQS].reshape(slot_count, -1)
    every_norm = pack_stats[:, REQS, :REQS].reshape(slot_count)
    logits = jnp.dot(
        every_last.astype(jnp.bfloat16), w_vocab, preferred_element_type=jnp.float32
    ) * logit_gain.astype(jnp.float32)
    every_max = lax.pmax(jnp.max(logits, axis=1), ("dp", "tensor"))
    placement = (pack_of_group[:, None] == jnp.arange(slot_count, dtype=jnp.int32)[None, :]).astype(
        jnp.float32
    )
    request_norm = jnp.dot(every_norm, placement, precision=lax.Precision.HIGHEST)
    max_logit = jnp.dot(every_max, placement, precision=lax.Precision.HIGHEST)
    return (result_rows[None], request_norm, max_logit)


def solution(mesh):
    return jax.shard_map(
        local,
        mesh=mesh,
        in_specs=(
            P("dp", "tensor", None),
            P("dp", "tensor"),
            P(),
            P(),
            P(),
            P(),
            P(),
            P(None, "dp"),
            P(None, "dp"),
            P("dp"),
            P("dp"),
            P("dp", None),
            P(),
            P(None, ("dp", "tensor")),
            P(("dp", "tensor")),
        ),
        out_specs=(P("dp", "tensor", None), P(), P()),
        check_vma=False,
    )
```

```python
import math

import jax
import jax.numpy as jnp
from jax import lax
from jax.sharding import PartitionSpec as P

HEADS = 10
HD = 64
REQS = 4


EPSILON = 1e-06
NEGATIVE = -1e30


def normalize(values):
    return values * lax.rsqrt(jnp.mean(values * values, axis=-1, keepdims=True) + EPSILON)


def head_norm(values, qk_gain):
    reshaped = values.reshape(values.shape[0], HEADS, HD)
    return (normalize(reshaped) * qk_gain.reshape(HEADS, HD)).astype(jnp.bfloat16)


def local(
    tokens,
    segment_ids,
    pack_of_group,
    w_qkv,
    qk_gain,
    w_out,
    alpha_attn,
    w_up,
    w_gate,
    up_gain,
    gate_gain,
    w_down,
    alpha_mlp,
    w_vocab,
    logit_gain,
):
    row_count = tokens.shape[1]
    head_width = HEADS * HD
    segments = segment_ids[0]
    tensor_index = lax.axis_index("tensor")
    positions = tensor_index * row_count + jnp.arange(row_count, dtype=jnp.int32)
    request_numbers = jnp.arange(REQS, dtype=jnp.int32)
    start_rows = normalize(tokens[0].astype(jnp.float32)).astype(jnp.bfloat16)
    projected = jnp.dot(start_rows, w_qkv, preferred_element_type=jnp.float32)
    queries = head_norm(projected[:, :head_width], qk_gain)
    key_rows = head_norm(projected[:, head_width : 2 * head_width], qk_gain).reshape(
        row_count, head_width
    )
    value_rows = projected[:, 2 * head_width :].astype(jnp.bfloat16)
    score_scale = 1.0 / math.sqrt(HD)
    seg_block = jnp.zeros((8, 2 * head_width), jnp.bfloat16).at[0, :row_count].set(
        segments.astype(jnp.bfloat16)
    )
    packed = jnp.concatenate(
        [jnp.concatenate([key_rows, value_rows], axis=1), seg_block], axis=0
    )
    gathered = lax.all_gather(packed, "tensor", axis=0, tiled=False)
    vocab_pack = jnp.concatenate(
        [w_vocab, logit_gain[None], jnp.zeros((7, w_vocab.shape[1]), w_vocab.dtype)], axis=0
    )
    vocab_pack, gathered = lax.optimization_barrier((vocab_pack, gathered))
    vocab_all = lax.all_gather(vocab_pack, "dp", axis=0, tiled=False)
    key_all = gathered[:, :row_count, :head_width].reshape(-1, head_width)
    value_all = gathered[:, :row_count, head_width:].reshape(-1, head_width)
    seg_all = gathered[:, row_count, :row_count].reshape(-1).astype(jnp.int32)
    tally = jnp.sum((seg_all[:, None] == request_numbers[None, :]).astype(jnp.int32), axis=0)
    total_keys = key_all.shape[0]
    key_pos = jnp.arange(total_keys, dtype=jnp.int32)
    head_of_column = jnp.arange(head_width, dtype=jnp.int32) // HD
    head_mask = (jnp.arange(HEADS, dtype=jnp.int32)[:, None] == head_of_column[None, :]).astype(
        jnp.bfloat16
    )
    query_flat = queries.reshape(row_count, head_width)
    query_blocks = (query_flat[None, :, :] * head_mask[:, None, :]).reshape(
        HEADS * row_count, head_width
    )
    scores = (
        lax.dot_general(
            query_blocks,
            key_all,
            (((1,), (1,)), ((), ())),
            preferred_element_type=jnp.float32,
        ).reshape(HEADS, row_count, total_keys)
        * score_scale
    )
    allowed = (seg_all[None, :] == segments[:, None]) & (key_pos[None, :] <= positions[:, None])
    row_max = jnp.max(jnp.where(allowed[None], scores, NEGATIVE), axis=2)
    weights = jnp.where(allowed[None], jnp.exp(scores - row_max[:, :, None]), 0.0)
    weight_sum = jnp.sum(weights, axis=2)
    weighted = jnp.dot(
        weights.astype(jnp.bfloat16).reshape(HEADS * row_count, total_keys),
        value_all,
        preferred_element_type=jnp.float32,
    ).reshape(HEADS, row_count, head_width)
    attended = jnp.sum(
        (weighted / weight_sum[:, :, None]) * head_mask[:, None, :].astype(jnp.float32), axis=0
    ).astype(jnp.bfloat16)
    attn_rows = normalize(jnp.dot(attended, w_out, preferred_element_type=jnp.float32))
    residual_in = start_rows.astype(jnp.float32)
    mid_rows = normalize(residual_in + alpha_attn * (attn_rows - residual_in)).astype(jnp.bfloat16)
    mid_rows, vocab_all = lax.optimization_barrier((mid_rows, vocab_all))
    received = lax.all_gather(mid_rows, "dp", axis=0, tiled=True)
    up_proj = jnp.dot(received, w_up, preferred_element_type=jnp.float32) * up_gain
    gate_proj = jnp.dot(received, w_gate, preferred_element_type=jnp.float32) * gate_gain
    hidden = (up_proj * jax.nn.silu(gate_proj)).astype(jnp.bfloat16)
    mixed_sum = lax.psum_scatter(
        jnp.dot(hidden, w_down, preferred_element_type=jnp.float32).astype(jnp.bfloat16),
        "dp",
        scatter_dimension=0,
        tiled=True,
    ).astype(jnp.float32)
    mlp_rows = normalize(mixed_sum)
    residual_mid = mid_rows.astype(jnp.float32)
    result_rows = normalize(residual_mid + alpha_mlp * (mlp_rows - residual_mid)).astype(
        jnp.bfloat16
    )
    request_ends = jnp.cumsum(tally) - 1
    same_request = segments[:, None] == request_numbers[None, :]
    row_end = jnp.sum(jnp.where(same_request, request_ends[None, :], 0), axis=1)
    is_last = positions == row_end
    member = same_request.astype(jnp.float32)
    chosen = member * is_last[:, None].astype(jnp.float32)
    result_f32 = result_rows.astype(jnp.float32)
    row_sums = jnp.dot(member.T, result_f32, precision=lax.Precision.HIGHEST)
    last_rows = jnp.dot(chosen.T, result_f32, precision=lax.Precision.HIGHEST)
    partial = jnp.concatenate([row_sums, last_rows], axis=0)
    summed = jnp.sum(lax.all_gather(partial, "tensor", axis=0, tiled=False), axis=0)
    row_sums, last_rows = summed[:REQS], summed[REQS:]
    counts = tally.astype(jnp.float32)
    request_mean = row_sums / counts[:, None]
    group_norm = jnp.sqrt(jnp.mean(request_mean * request_mean, axis=1))
    slot_count = lax.axis_size("dp") * REQS
    dp_index = lax.axis_index("dp")
    model_width = last_rows.shape[1]
    pack_logits = jnp.einsum(
        "rd,gdc->rgc",
        last_rows.astype(jnp.bfloat16),
        vocab_all[:, :model_width],
        preferred_element_type=jnp.float32,
    ) * vocab_all[None, :, model_width].astype(jnp.float32)
    pack_max = jnp.max(pack_logits.reshape(REQS, -1), axis=1)
    own_slot = jnp.arange(slot_count, dtype=jnp.int32) // REQS == dp_index
    spread_max = jnp.where(own_slot, jnp.tile(pack_max, slot_count // REQS), NEGATIVE)
    spread_norm = jnp.where(own_slot, jnp.tile(group_norm, slot_count // REQS), NEGATIVE)
    every = lax.pmax(jnp.concatenate([spread_max, spread_norm]), ("dp", "tensor"))
    every_max, every_norm = every[:slot_count], every[slot_count:]
    placement = (pack_of_group[:, None] == jnp.arange(slot_count, dtype=jnp.int32)[None, :]).astype(
        jnp.float32
    )
    request_norm = jnp.dot(every_norm, placement, precision=lax.Precision.HIGHEST)
    max_logit = jnp.dot(every_max, placement, precision=lax.Precision.HIGHEST)
    return (result_rows[None], request_norm, max_logit)


def solution(mesh):
    return jax.shard_map(
        local,
        mesh=mesh,
        in_specs=(
            P("dp", "tensor", None),
            P("dp", "tensor"),
            P(),
            P(),
            P(),
            P(),
            P(),
            P(None, "dp"),
            P(None, "dp"),
            P("dp"),
            P("dp"),
            P("dp", None),
            P(),
            P(None, ("dp", "tensor")),
            P(("dp", "tensor")),
        ),
        out_specs=(P("dp", "tensor", None), P(), P()),
        check_vma=False,
    )
```

```python
import math

import jax
import jax.numpy as jnp
from jax import lax
from jax.sharding import PartitionSpec as P

HEADS = 10
HD = 64
REQS = 4


EPSILON = 1e-06
NEGATIVE = -1e30


def normalize(values):
    return values * lax.rsqrt(jnp.mean(values * values, axis=-1, keepdims=True) + EPSILON)


def head_norm(values, qk_gain):
    reshaped = values.reshape(values.shape[0], HEADS, HD)
    return (normalize(reshaped) * qk_gain.reshape(HEADS, HD)).astype(jnp.bfloat16)


def local(
    tokens,
    segment_ids,
    pack_of_group,
    w_qkv,
    qk_gain,
    w_out,
    alpha_attn,
    w_up,
    w_gate,
    up_gain,
    gate_gain,
    w_down,
    alpha_mlp,
    w_vocab,
    logit_gain,
):
    row_count = tokens.shape[1]
    head_width = HEADS * HD
    segments = segment_ids[0]
    tensor_index = lax.axis_index("tensor")
    positions = tensor_index * row_count + jnp.arange(row_count, dtype=jnp.int32)
    request_numbers = jnp.arange(REQS, dtype=jnp.int32)
    start_rows = normalize(tokens[0].astype(jnp.float32)).astype(jnp.bfloat16)
    projected = jnp.dot(start_rows, w_qkv, preferred_element_type=jnp.float32)
    queries = head_norm(projected[:, :head_width], qk_gain)
    key_rows = head_norm(projected[:, head_width : 2 * head_width], qk_gain).reshape(
        row_count, head_width
    )
    value_rows = projected[:, 2 * head_width :].astype(jnp.bfloat16)
    score_scale = 1.0 / math.sqrt(HD)
    seg_block = jnp.zeros((8, 2 * head_width), jnp.bfloat16).at[0, :row_count].set(
        segments.astype(jnp.bfloat16)
    )
    packed = jnp.concatenate(
        [jnp.concatenate([key_rows, value_rows], axis=1), seg_block], axis=0
    )
    gathered = lax.all_gather(packed, "tensor", axis=0, tiled=False)
    vocab_pack = jnp.concatenate(
        [w_vocab, logit_gain[None], jnp.zeros((7, w_vocab.shape[1]), w_vocab.dtype)], axis=0
    )
    vocab_pack, gathered = lax.optimization_barrier((vocab_pack, gathered))
    vocab_all = lax.all_gather(vocab_pack, "dp", axis=0, tiled=False)
    key_all = gathered[:, :row_count, :head_width].reshape(-1, head_width)
    value_all = gathered[:, :row_count, head_width:].reshape(-1, head_width)
    seg_all = gathered[:, row_count, :row_count].reshape(-1).astype(jnp.int32)
    tally = jnp.sum((seg_all[:, None] == request_numbers[None, :]).astype(jnp.int32), axis=0)
    total_keys = key_all.shape[0]
    key_pos = jnp.arange(total_keys, dtype=jnp.int32)
    head_of_column = jnp.arange(head_width, dtype=jnp.int32) // HD
    head_mask = (jnp.arange(HEADS, dtype=jnp.int32)[:, None] == head_of_column[None, :]).astype(
        jnp.bfloat16
    )
    query_flat = queries.reshape(row_count, head_width)
    query_blocks = (query_flat[None, :, :] * head_mask[:, None, :]).reshape(
        HEADS * row_count, head_width
    )
    scores = (
        lax.dot_general(
            query_blocks,
            key_all,
            (((1,), (1,)), ((), ())),
            preferred_element_type=jnp.float32,
        ).reshape(HEADS, row_count, total_keys)
        * score_scale
    )
    allowed = (seg_all[None, :] == segments[:, None]) & (key_pos[None, :] <= positions[:, None])
    row_max = jnp.max(jnp.where(allowed[None], scores, NEGATIVE), axis=2)
    weights = jnp.where(allowed[None], jnp.exp(scores - row_max[:, :, None]), 0.0)
    weight_sum = jnp.sum(weights, axis=2)
    weighted = jnp.dot(
        weights.astype(jnp.bfloat16).reshape(HEADS * row_count, total_keys),
        value_all,
        preferred_element_type=jnp.float32,
    ).reshape(HEADS, row_count, head_width)
    attended = jnp.sum(
        (weighted / weight_sum[:, :, None]) * head_mask[:, None, :].astype(jnp.float32), axis=0
    ).astype(jnp.bfloat16)
    attn_rows = normalize(jnp.dot(attended, w_out, preferred_element_type=jnp.float32))
    residual_in = start_rows.astype(jnp.float32)
    mid_rows = normalize(residual_in + alpha_attn * (attn_rows - residual_in)).astype(jnp.bfloat16)
    mid_rows, vocab_all = lax.optimization_barrier((mid_rows, vocab_all))
    received = lax.all_gather(mid_rows, "dp", axis=0, tiled=True)
    up_proj = jnp.dot(received, w_up, preferred_element_type=jnp.float32) * up_gain
    gate_proj = jnp.dot(received, w_gate, preferred_element_type=jnp.float32) * gate_gain
    hidden = (up_proj * jax.nn.silu(gate_proj)).astype(jnp.bfloat16)
    mixed_sum = lax.psum_scatter(
        jnp.dot(hidden, w_down, preferred_element_type=jnp.float32).astype(jnp.bfloat16),
        "dp",
        scatter_dimension=0,
        tiled=True,
    ).astype(jnp.float32)
    mlp_rows = normalize(mixed_sum)
    residual_mid = mid_rows.astype(jnp.float32)
    result_rows = normalize(residual_mid + alpha_mlp * (mlp_rows - residual_mid)).astype(
        jnp.bfloat16
    )
    request_ends = jnp.cumsum(tally) - 1
    same_request = segments[:, None] == request_numbers[None, :]
    row_end = jnp.sum(jnp.where(same_request, request_ends[None, :], 0), axis=1)
    is_last = positions == row_end
    member = same_request.astype(jnp.float32)
    chosen = member * is_last[:, None].astype(jnp.float32)
    result_f32 = result_rows.astype(jnp.float32)
    row_sums = jnp.dot(member.T, result_f32, precision=lax.Precision.HIGHEST)
    last_rows = jnp.dot(chosen.T, result_f32, precision=lax.Precision.HIGHEST)
    partial = jnp.concatenate([row_sums, last_rows], axis=0)
    summed = jnp.sum(
        lax.all_gather(partial.astype(jnp.bfloat16), "tensor", axis=0, tiled=False).astype(
            jnp.float32
        ),
        axis=0,
    )
    row_sums, last_rows = summed[:REQS], summed[REQS:]
    counts = tally.astype(jnp.float32)
    request_mean = row_sums / counts[:, None]
    group_norm = jnp.sqrt(jnp.mean(request_mean * request_mean, axis=1))
    slot_count = lax.axis_size("dp") * REQS
    dp_index = lax.axis_index("dp")
    model_width = last_rows.shape[1]
    pack_logits = jnp.einsum(
        "rd,gdc->rgc",
        last_rows.astype(jnp.bfloat16),
        vocab_all[:, :model_width],
        preferred_element_type=jnp.float32,
    ) * vocab_all[None, :, model_width].astype(jnp.float32)
    pack_max = jnp.max(pack_logits.reshape(REQS, -1), axis=1)
    own_slot = jnp.arange(slot_count, dtype=jnp.int32) // REQS == dp_index
    spread_max = jnp.where(own_slot, jnp.tile(pack_max, slot_count // REQS), NEGATIVE)
    spread_norm = jnp.where(own_slot, jnp.tile(group_norm, slot_count // REQS), NEGATIVE)
    every = lax.pmax(jnp.concatenate([spread_max, spread_norm]), ("dp", "tensor"))
    every_max, every_norm = every[:slot_count], every[slot_count:]
    placement = (pack_of_group[:, None] == jnp.arange(slot_count, dtype=jnp.int32)[None, :]).astype(
        jnp.float32
    )
    request_norm = jnp.dot(every_norm, placement, precision=lax.Precision.HIGHEST)
    max_logit = jnp.dot(every_max, placement, precision=lax.Precision.HIGHEST)
    return (result_rows[None], request_norm, max_logit)


def solution(mesh):
    return jax.shard_map(
        local,
        mesh=mesh,
        in_specs=(
            P("dp", "tensor", None),
            P("dp", "tensor"),
            P(),
            P(),
            P(),
            P(),
            P(),
            P(None, "dp"),
            P(None, "dp"),
            P("dp"),
            P("dp"),
            P("dp", None),
            P(),
            P(None, ("dp", "tensor")),
            P(("dp", "tensor")),
        ),
        out_specs=(P("dp", "tensor", None), P(), P()),
        check_vma=False,
    )
```

```python
import math

import jax
import jax.numpy as jnp
from jax import lax
from jax.sharding import PartitionSpec as P

HEADS = 10
HD = 64
REQS = 4


EPSILON = 1e-06
NEGATIVE = -1e30


def normalize(values):
    return values * lax.rsqrt(jnp.mean(values * values, axis=-1, keepdims=True) + EPSILON)


def head_norm(values, qk_gain):
    reshaped = values.reshape(values.shape[0], HEADS, HD)
    return (normalize(reshaped) * qk_gain.reshape(HEADS, HD)).astype(jnp.bfloat16)


def local(
    tokens,
    segment_ids,
    pack_of_group,
    w_qkv,
    qk_gain,
    w_out,
    alpha_attn,
    w_up,
    w_gate,
    up_gain,
    gate_gain,
    w_down,
    alpha_mlp,
    w_vocab,
    logit_gain,
):
    row_count = tokens.shape[1]
    head_width = HEADS * HD
    segments = segment_ids[0]
    tensor_index = lax.axis_index("tensor")
    positions = tensor_index * row_count + jnp.arange(row_count, dtype=jnp.int32)
    request_numbers = jnp.arange(REQS, dtype=jnp.int32)
    start_rows = normalize(tokens[0].astype(jnp.float32)).astype(jnp.bfloat16)
    projected = jnp.dot(start_rows, w_qkv, preferred_element_type=jnp.float32)
    queries = head_norm(projected[:, :head_width], qk_gain)
    key_rows = head_norm(projected[:, head_width : 2 * head_width], qk_gain).reshape(
        row_count, head_width
    )
    value_rows = projected[:, 2 * head_width :].astype(jnp.bfloat16)
    score_scale = 1.0 / math.sqrt(HD)
    seg_block = jnp.zeros((8, 2 * head_width), jnp.bfloat16).at[0, :row_count].set(
        segments.astype(jnp.bfloat16)
    )
    packed = jnp.concatenate(
        [jnp.concatenate([key_rows, value_rows], axis=1), seg_block], axis=0
    )
    gathered = lax.all_gather(packed, "tensor", axis=0, tiled=False)
    vocab_pack = jnp.concatenate(
        [w_vocab, logit_gain[None], jnp.zeros((7, w_vocab.shape[1]), w_vocab.dtype)], axis=0
    )
    dp_size = lax.axis_size("dp")
    vocab_all = jnp.stack(
        [vocab_pack]
        + [
            lax.ppermute(vocab_pack, "dp", [(i, (i + shift) % dp_size) for i in range(dp_size)])
            for shift in range(1, dp_size)
        ]
    )
    key_all = gathered[:, :row_count, :head_width].reshape(-1, head_width)
    value_all = gathered[:, :row_count, head_width:].reshape(-1, head_width)
    seg_all = gathered[:, row_count, :row_count].reshape(-1).astype(jnp.int32)
    tally = jnp.sum((seg_all[:, None] == request_numbers[None, :]).astype(jnp.int32), axis=0)
    total_keys = key_all.shape[0]
    key_pos = jnp.arange(total_keys, dtype=jnp.int32)
    head_of_column = jnp.arange(head_width, dtype=jnp.int32) // HD
    head_mask = (jnp.arange(HEADS, dtype=jnp.int32)[:, None] == head_of_column[None, :]).astype(
        jnp.bfloat16
    )
    query_flat = queries.reshape(row_count, head_width)
    query_blocks = (query_flat[None, :, :] * head_mask[:, None, :]).reshape(
        HEADS * row_count, head_width
    )
    scores = (
        lax.dot_general(
            query_blocks,
            key_all,
            (((1,), (1,)), ((), ())),
            preferred_element_type=jnp.float32,
        ).reshape(HEADS, row_count, total_keys)
        * score_scale
    )
    allowed = (seg_all[None, :] == segments[:, None]) & (key_pos[None, :] <= positions[:, None])
    row_max = jnp.max(jnp.where(allowed[None], scores, NEGATIVE), axis=2)
    weights = jnp.where(allowed[None], jnp.exp(scores - row_max[:, :, None]), 0.0)
    weight_sum = jnp.sum(weights, axis=2)
    weighted = jnp.dot(
        weights.astype(jnp.bfloat16).reshape(HEADS * row_count, total_keys),
        value_all,
        preferred_element_type=jnp.float32,
    ).reshape(HEADS, row_count, head_width)
    attended = jnp.sum(
        (weighted / weight_sum[:, :, None]) * head_mask[:, None, :].astype(jnp.float32), axis=0
    ).astype(jnp.bfloat16)
    attn_rows = normalize(jnp.dot(attended, w_out, preferred_element_type=jnp.float32))
    residual_in = start_rows.astype(jnp.float32)
    mid_rows = normalize(residual_in + alpha_attn * (attn_rows - residual_in)).astype(jnp.bfloat16)
    mid_rows, vocab_all = lax.optimization_barrier((mid_rows, vocab_all))
    received = lax.all_gather(mid_rows, "dp", axis=0, tiled=True)
    up_proj = jnp.dot(received, w_up, preferred_element_type=jnp.float32) * up_gain
    gate_proj = jnp.dot(received, w_gate, preferred_element_type=jnp.float32) * gate_gain
    hidden = (up_proj * jax.nn.silu(gate_proj)).astype(jnp.bfloat16)
    mixed_sum = lax.psum_scatter(
        jnp.dot(hidden, w_down, preferred_element_type=jnp.float32).astype(jnp.bfloat16),
        "dp",
        scatter_dimension=0,
        tiled=True,
    ).astype(jnp.float32)
    mlp_rows = normalize(mixed_sum)
    residual_mid = mid_rows.astype(jnp.float32)
    result_rows = normalize(residual_mid + alpha_mlp * (mlp_rows - residual_mid)).astype(
        jnp.bfloat16
    )
    request_ends = jnp.cumsum(tally) - 1
    same_request = segments[:, None] == request_numbers[None, :]
    row_end = jnp.sum(jnp.where(same_request, request_ends[None, :], 0), axis=1)
    is_last = positions == row_end
    member = same_request.astype(jnp.float32)
    chosen = member * is_last[:, None].astype(jnp.float32)
    result_f32 = result_rows.astype(jnp.float32)
    row_sums = jnp.dot(member.T, result_f32, precision=lax.Precision.HIGHEST)
    last_rows = jnp.dot(chosen.T, result_f32, precision=lax.Precision.HIGHEST)
    partial = jnp.concatenate([row_sums, last_rows], axis=0)
    summed = jnp.sum(
        lax.all_gather(partial.astype(jnp.bfloat16), "tensor", axis=0, tiled=False).astype(
            jnp.float32
        ),
        axis=0,
    )
    row_sums, last_rows = summed[:REQS], summed[REQS:]
    counts = tally.astype(jnp.float32)
    request_mean = row_sums / counts[:, None]
    group_norm = jnp.sqrt(jnp.mean(request_mean * request_mean, axis=1))
    slot_count = lax.axis_size("dp") * REQS
    dp_index = lax.axis_index("dp")
    model_width = last_rows.shape[1]
    pack_logits = jnp.einsum(
        "rd,gdc->rgc",
        last_rows.astype(jnp.bfloat16),
        vocab_all[:, :model_width],
        preferred_element_type=jnp.float32,
    ) * vocab_all[None, :, model_width].astype(jnp.float32)
    pack_max = jnp.max(pack_logits.reshape(REQS, -1), axis=1)
    own_slot = jnp.arange(slot_count, dtype=jnp.int32) // REQS == dp_index
    spread_max = jnp.where(own_slot, jnp.tile(pack_max, slot_count // REQS), NEGATIVE)
    spread_norm = jnp.where(own_slot, jnp.tile(group_norm, slot_count // REQS), NEGATIVE)
    every = lax.pmax(jnp.concatenate([spread_max, spread_norm]), ("dp", "tensor"))
    every_max, every_norm = every[:slot_count], every[slot_count:]
    placement = (pack_of_group[:, None] == jnp.arange(slot_count, dtype=jnp.int32)[None, :]).astype(
        jnp.float32
    )
    request_norm = jnp.dot(every_norm, placement, precision=lax.Precision.HIGHEST)
    max_logit = jnp.dot(every_max, placement, precision=lax.Precision.HIGHEST)
    return (result_rows[None], request_norm, max_logit)


def solution(mesh):
    return jax.shard_map(
        local,
        mesh=mesh,
        in_specs=(
            P("dp", "tensor", None),
            P("dp", "tensor"),
            P(),
            P(),
            P(),
            P(),
            P(),
            P(None, "dp"),
            P(None, "dp"),
            P("dp"),
            P("dp"),
            P("dp", None),
            P(),
            P(None, ("dp", "tensor")),
            P(("dp", "tensor")),
        ),
        out_specs=(P("dp", "tensor", None), P(), P()),
        check_vma=False,
    )
```

```python
import math

import jax
import jax.numpy as jnp
from jax import lax
from jax.sharding import PartitionSpec as P

HEADS = 10
HD = 64
REQS = 4


EPSILON = 1e-06
NEGATIVE = -1e30


def normalize(values):
    return values * lax.rsqrt(jnp.mean(values * values, axis=-1, keepdims=True) + EPSILON)


def head_norm(values, qk_gain):
    reshaped = values.reshape(values.shape[0], HEADS, HD)
    return (normalize(reshaped) * qk_gain.reshape(HEADS, HD)).astype(jnp.bfloat16)


def local(
    tokens,
    segment_ids,
    pack_of_group,
    w_qkv,
    qk_gain,
    w_out,
    alpha_attn,
    w_up,
    w_gate,
    up_gain,
    gate_gain,
    w_down,
    alpha_mlp,
    w_vocab,
    logit_gain,
):
    row_count = tokens.shape[1]
    head_width = HEADS * HD
    segments = segment_ids[0]
    tensor_index = lax.axis_index("tensor")
    positions = tensor_index * row_count + jnp.arange(row_count, dtype=jnp.int32)
    request_numbers = jnp.arange(REQS, dtype=jnp.int32)
    start_rows = normalize(tokens[0].astype(jnp.float32)).astype(jnp.bfloat16)
    projected = jnp.dot(start_rows, w_qkv, preferred_element_type=jnp.float32)
    queries = head_norm(projected[:, :head_width], qk_gain)
    key_rows = head_norm(projected[:, head_width : 2 * head_width], qk_gain).reshape(
        row_count, head_width
    )
    value_rows = projected[:, 2 * head_width :].astype(jnp.bfloat16)
    score_scale = 1.0 / math.sqrt(HD)
    seg_block = jnp.zeros((8, 2 * head_width), jnp.bfloat16).at[0, :row_count].set(
        segments.astype(jnp.bfloat16)
    )
    packed = jnp.concatenate(
        [jnp.concatenate([key_rows, value_rows], axis=1), seg_block], axis=0
    )
    gathered = lax.all_gather(packed, "tensor", axis=0, tiled=False)
    vocab_pack = jnp.concatenate(
        [w_vocab, logit_gain[None], jnp.zeros((7, w_vocab.shape[1]), w_vocab.dtype)], axis=0
    )
    vocab_pack, gathered = lax.optimization_barrier((vocab_pack, gathered))
    dp_size = lax.axis_size("dp")
    vocab_all = jnp.stack(
        [vocab_pack]
        + [
            lax.ppermute(vocab_pack, "dp", [(i, (i + shift) % dp_size) for i in range(dp_size)])
            for shift in range(1, dp_size)
        ]
    )
    key_all = gathered[:, :row_count, :head_width].reshape(-1, head_width)
    value_all = gathered[:, :row_count, head_width:].reshape(-1, head_width)
    seg_all = gathered[:, row_count, :row_count].reshape(-1).astype(jnp.int32)
    tally = jnp.sum((seg_all[:, None] == request_numbers[None, :]).astype(jnp.int32), axis=0)
    total_keys = key_all.shape[0]
    key_pos = jnp.arange(total_keys, dtype=jnp.int32)
    head_of_column = jnp.arange(head_width, dtype=jnp.int32) // HD
    head_mask = (jnp.arange(HEADS, dtype=jnp.int32)[:, None] == head_of_column[None, :]).astype(
        jnp.bfloat16
    )
    query_flat = queries.reshape(row_count, head_width)
    query_blocks = (query_flat[None, :, :] * head_mask[:, None, :]).reshape(
        HEADS * row_count, head_width
    )
    scores = (
        lax.dot_general(
            query_blocks,
            key_all,
            (((1,), (1,)), ((), ())),
            preferred_element_type=jnp.float32,
        ).reshape(HEADS, row_count, total_keys)
        * score_scale
    )
    allowed = (seg_all[None, :] == segments[:, None]) & (key_pos[None, :] <= positions[:, None])
    row_max = jnp.max(jnp.where(allowed[None], scores, NEGATIVE), axis=2)
    weights = jnp.where(allowed[None], jnp.exp(scores - row_max[:, :, None]), 0.0)
    weight_sum = jnp.sum(weights, axis=2)
    weighted = jnp.dot(
        weights.astype(jnp.bfloat16).reshape(HEADS * row_count, total_keys),
        value_all,
        preferred_element_type=jnp.float32,
    ).reshape(HEADS, row_count, head_width)
    attended = jnp.sum(
        (weighted / weight_sum[:, :, None]) * head_mask[:, None, :].astype(jnp.float32), axis=0
    ).astype(jnp.bfloat16)
    attn_rows = normalize(jnp.dot(attended, w_out, preferred_element_type=jnp.float32))
    residual_in = start_rows.astype(jnp.float32)
    mid_rows = normalize(residual_in + alpha_attn * (attn_rows - residual_in)).astype(jnp.bfloat16)
    mid_rows, vocab_all = lax.optimization_barrier((mid_rows, vocab_all))
    received = lax.all_gather(mid_rows, "dp", axis=0, tiled=True)
    up_proj = jnp.dot(received, w_up, preferred_element_type=jnp.float32) * up_gain
    gate_proj = jnp.dot(received, w_gate, preferred_element_type=jnp.float32) * gate_gain
    hidden = (up_proj * jax.nn.silu(gate_proj)).astype(jnp.bfloat16)
    mixed_sum = lax.psum_scatter(
        jnp.dot(hidden, w_down, preferred_element_type=jnp.float32).astype(jnp.bfloat16),
        "dp",
        scatter_dimension=0,
        tiled=True,
    ).astype(jnp.float32)
    mlp_rows = normalize(mixed_sum)
    residual_mid = mid_rows.astype(jnp.float32)
    result_rows = normalize(residual_mid + alpha_mlp * (mlp_rows - residual_mid)).astype(
        jnp.bfloat16
    )
    request_ends = jnp.cumsum(tally) - 1
    same_request = segments[:, None] == request_numbers[None, :]
    row_end = jnp.sum(jnp.where(same_request, request_ends[None, :], 0), axis=1)
    is_last = positions == row_end
    member = same_request.astype(jnp.float32)
    chosen = member * is_last[:, None].astype(jnp.float32)
    result_f32 = result_rows.astype(jnp.float32)
    row_sums = jnp.dot(member.T, result_f32, precision=lax.Precision.HIGHEST)
    last_rows = jnp.dot(chosen.T, result_f32, precision=lax.Precision.HIGHEST)
    partial = jnp.concatenate([row_sums, last_rows], axis=0)
    summed = jnp.sum(
        lax.all_gather(partial.astype(jnp.bfloat16), "tensor", axis=0, tiled=False).astype(
            jnp.float32
        ),
        axis=0,
    )
    row_sums, last_rows = summed[:REQS], summed[REQS:]
    counts = tally.astype(jnp.float32)
    request_mean = row_sums / counts[:, None]
    group_norm = jnp.sqrt(jnp.mean(request_mean * request_mean, axis=1))
    slot_count = lax.axis_size("dp") * REQS
    dp_index = lax.axis_index("dp")
    model_width = last_rows.shape[1]
    pack_logits = jnp.einsum(
        "rd,gdc->rgc",
        last_rows.astype(jnp.bfloat16),
        vocab_all[:, :model_width],
        preferred_element_type=jnp.float32,
    ) * vocab_all[None, :, model_width].astype(jnp.float32)
    pack_max = jnp.max(pack_logits.reshape(REQS, -1), axis=1)
    own_slot = jnp.arange(slot_count, dtype=jnp.int32) // REQS == dp_index
    spread_max = jnp.where(own_slot, jnp.tile(pack_max, slot_count // REQS), NEGATIVE)
    spread_norm = jnp.where(own_slot, jnp.tile(group_norm, slot_count // REQS), NEGATIVE)
    every = lax.pmax(jnp.concatenate([spread_max, spread_norm]), ("dp", "tensor"))
    every_max, every_norm = every[:slot_count], every[slot_count:]
    placement = (pack_of_group[:, None] == jnp.arange(slot_count, dtype=jnp.int32)[None, :]).astype(
        jnp.float32
    )
    request_norm = jnp.dot(every_norm, placement, precision=lax.Precision.HIGHEST)
    max_logit = jnp.dot(every_max, placement, precision=lax.Precision.HIGHEST)
    return (result_rows[None], request_norm, max_logit)


def solution(mesh):
    return jax.shard_map(
        local,
        mesh=mesh,
        in_specs=(
            P("dp", "tensor", None),
            P("dp", "tensor"),
            P(),
            P(),
            P(),
            P(),
            P(),
            P(None, "dp"),
            P(None, "dp"),
            P("dp"),
            P("dp"),
            P("dp", None),
            P(),
            P(None, ("dp", "tensor")),
            P(("dp", "tensor")),
        ),
        out_specs=(P("dp", "tensor", None), P(), P()),
        check_vma=False,
    )
```

```python
import math

import jax
import jax.numpy as jnp
from jax import lax
from jax.sharding import PartitionSpec as P

HEADS = 10
HD = 64
REQS = 4


EPSILON = 1e-06
NEGATIVE = -1e30


def normalize(values):
    return values * lax.rsqrt(jnp.mean(values * values, axis=-1, keepdims=True) + EPSILON)


def head_norm(values, qk_gain):
    reshaped = values.reshape(values.shape[0], HEADS, HD)
    return (normalize(reshaped) * qk_gain.reshape(HEADS, HD)).astype(jnp.bfloat16)


def local(
    tokens,
    segment_ids,
    pack_of_group,
    w_qkv,
    qk_gain,
    w_out,
    alpha_attn,
    w_up,
    w_gate,
    up_gain,
    gate_gain,
    w_down,
    alpha_mlp,
    w_vocab,
    logit_gain,
):
    row_count = tokens.shape[1]
    head_width = HEADS * HD
    segments = segment_ids[0]
    tensor_index = lax.axis_index("tensor")
    positions = tensor_index * row_count + jnp.arange(row_count, dtype=jnp.int32)
    request_numbers = jnp.arange(REQS, dtype=jnp.int32)
    start_rows = normalize(tokens[0].astype(jnp.float32)).astype(jnp.bfloat16)
    projected = jnp.dot(start_rows, w_qkv, preferred_element_type=jnp.float32)
    queries = head_norm(projected[:, :head_width], qk_gain)
    key_rows = head_norm(projected[:, head_width : 2 * head_width], qk_gain).reshape(
        row_count, head_width
    )
    value_rows = projected[:, 2 * head_width :].astype(jnp.bfloat16)
    score_scale = 1.0 / math.sqrt(HD)
    packed = jnp.concatenate([key_rows, value_rows], axis=1)
    gathered = lax.all_gather(packed, "tensor", axis=0, tiled=False)
    vocab_pack = jnp.concatenate(
        [w_vocab, logit_gain[None], jnp.zeros((7, w_vocab.shape[1]), w_vocab.dtype)], axis=0
    )
    vocab_pack, gathered = lax.optimization_barrier((vocab_pack, gathered))
    vocab_all = lax.all_gather(vocab_pack, "dp", axis=0, tiled=False)
    key_all = gathered[:, :row_count, :head_width].reshape(-1, head_width)
    value_all = gathered[:, :row_count, head_width:].reshape(-1, head_width)
    seg_all = lax.all_gather(segments, "tensor", axis=0, tiled=True)
    tally = jnp.sum((seg_all[:, None] == request_numbers[None, :]).astype(jnp.int32), axis=0)
    total_keys = key_all.shape[0]
    key_pos = jnp.arange(total_keys, dtype=jnp.int32)
    head_of_column = jnp.arange(head_width, dtype=jnp.int32) // HD
    head_mask = (jnp.arange(HEADS, dtype=jnp.int32)[:, None] == head_of_column[None, :]).astype(
        jnp.bfloat16
    )
    query_flat = queries.reshape(row_count, head_width)
    query_blocks = (query_flat[None, :, :] * head_mask[:, None, :]).reshape(
        HEADS * row_count, head_width
    )
    scores = (
        lax.dot_general(
            query_blocks,
            key_all,
            (((1,), (1,)), ((), ())),
            preferred_element_type=jnp.float32,
        ).reshape(HEADS, row_count, total_keys)
        * score_scale
    )
    allowed = (seg_all[None, :] == segments[:, None]) & (key_pos[None, :] <= positions[:, None])
    row_max = jnp.max(jnp.where(allowed[None], scores, NEGATIVE), axis=2)
    weights = jnp.where(allowed[None], jnp.exp(scores - row_max[:, :, None]), 0.0)
    weight_sum = jnp.sum(weights, axis=2)
    weighted = jnp.dot(
        weights.astype(jnp.bfloat16).reshape(HEADS * row_count, total_keys),
        value_all,
        preferred_element_type=jnp.float32,
    ).reshape(HEADS, row_count, head_width)
    attended = jnp.sum(
        (weighted / weight_sum[:, :, None]) * head_mask[:, None, :].astype(jnp.float32), axis=0
    ).astype(jnp.bfloat16)
    attn_rows = normalize(jnp.dot(attended, w_out, preferred_element_type=jnp.float32))
    residual_in = start_rows.astype(jnp.float32)
    mid_rows = normalize(residual_in + alpha_attn * (attn_rows - residual_in)).astype(jnp.bfloat16)
    mid_rows, vocab_all = lax.optimization_barrier((mid_rows, vocab_all))
    received = lax.all_gather(mid_rows, "dp", axis=0, tiled=True)
    up_proj = jnp.dot(received, w_up, preferred_element_type=jnp.float32) * up_gain
    gate_proj = jnp.dot(received, w_gate, preferred_element_type=jnp.float32) * gate_gain
    hidden = (up_proj * jax.nn.silu(gate_proj)).astype(jnp.bfloat16)
    mixed_sum = lax.psum_scatter(
        jnp.dot(hidden, w_down, preferred_element_type=jnp.float32).astype(jnp.bfloat16),
        "dp",
        scatter_dimension=0,
        tiled=True,
    ).astype(jnp.float32)
    mlp_rows = normalize(mixed_sum)
    residual_mid = mid_rows.astype(jnp.float32)
    result_rows = normalize(residual_mid + alpha_mlp * (mlp_rows - residual_mid)).astype(
        jnp.bfloat16
    )
    request_ends = jnp.cumsum(tally) - 1
    same_request = segments[:, None] == request_numbers[None, :]
    row_end = jnp.sum(jnp.where(same_request, request_ends[None, :], 0), axis=1)
    is_last = positions == row_end
    member = same_request.astype(jnp.float32)
    chosen = member * is_last[:, None].astype(jnp.float32)
    result_f32 = result_rows.astype(jnp.float32)
    row_sums = jnp.dot(member.T, result_f32, precision=lax.Precision.HIGHEST)
    last_rows = jnp.dot(chosen.T, result_f32, precision=lax.Precision.HIGHEST)
    partial = jnp.concatenate([row_sums, last_rows], axis=0)
    summed = jnp.sum(
        lax.all_gather(partial.astype(jnp.bfloat16), "tensor", axis=0, tiled=False).astype(
            jnp.float32
        ),
        axis=0,
    )
    row_sums, last_rows = summed[:REQS], summed[REQS:]
    counts = tally.astype(jnp.float32)
    request_mean = row_sums / counts[:, None]
    group_norm = jnp.sqrt(jnp.mean(request_mean * request_mean, axis=1))
    slot_count = lax.axis_size("dp") * REQS
    dp_index = lax.axis_index("dp")
    model_width = last_rows.shape[1]
    pack_logits = jnp.einsum(
        "rd,gdc->rgc",
        last_rows.astype(jnp.bfloat16),
        vocab_all[:, :model_width],
        preferred_element_type=jnp.float32,
    ) * vocab_all[None, :, model_width].astype(jnp.float32)
    pack_max = jnp.max(pack_logits.reshape(REQS, -1), axis=1)
    own_slot = jnp.arange(slot_count, dtype=jnp.int32) // REQS == dp_index
    spread_max = jnp.where(own_slot, jnp.tile(pack_max, slot_count // REQS), NEGATIVE)
    spread_norm = jnp.where(own_slot, jnp.tile(group_norm, slot_count // REQS), NEGATIVE)
    every = lax.pmax(jnp.concatenate([spread_max, spread_norm]), ("dp", "tensor"))
    every_max, every_norm = every[:slot_count], every[slot_count:]
    placement = (pack_of_group[:, None] == jnp.arange(slot_count, dtype=jnp.int32)[None, :]).astype(
        jnp.float32
    )
    request_norm = jnp.dot(every_norm, placement, precision=lax.Precision.HIGHEST)
    max_logit = jnp.dot(every_max, placement, precision=lax.Precision.HIGHEST)
    return (result_rows[None], request_norm, max_logit)


def solution(mesh):
    return jax.shard_map(
        local,
        mesh=mesh,
        in_specs=(
            P("dp", "tensor", None),
            P("dp", "tensor"),
            P(),
            P(),
            P(),
            P(),
            P(),
            P(None, "dp"),
            P(None, "dp"),
            P("dp"),
            P("dp"),
            P("dp", None),
            P(),
            P(None, ("dp", "tensor")),
            P(("dp", "tensor")),
        ),
        out_specs=(P("dp", "tensor", None), P(), P()),
        check_vma=False,
    )
```

```python
import math

import jax
import jax.numpy as jnp
from jax import lax
from jax.sharding import PartitionSpec as P

HEADS = 10
HD = 64
REQS = 4


EPSILON = 1e-06
NEGATIVE = -1e30


def normalize(values):
    return values * lax.rsqrt(jnp.mean(values * values, axis=-1, keepdims=True) + EPSILON)


def head_norm(values, qk_gain):
    reshaped = values.reshape(values.shape[0], HEADS, HD)
    return (normalize(reshaped) * qk_gain.reshape(HEADS, HD)).astype(jnp.bfloat16)


def local(
    tokens,
    segment_ids,
    pack_of_group,
    w_qkv,
    qk_gain,
    w_out,
    alpha_attn,
    w_up,
    w_gate,
    up_gain,
    gate_gain,
    w_down,
    alpha_mlp,
    w_vocab,
    logit_gain,
):
    row_count = tokens.shape[1]
    head_width = HEADS * HD
    segments = segment_ids[0]
    tensor_index = lax.axis_index("tensor")
    positions = tensor_index * row_count + jnp.arange(row_count, dtype=jnp.int32)
    request_numbers = jnp.arange(REQS, dtype=jnp.int32)
    start_rows = normalize(tokens[0].astype(jnp.float32)).astype(jnp.bfloat16)
    projected = jnp.dot(start_rows, w_qkv, preferred_element_type=jnp.float32)
    queries = head_norm(projected[:, :head_width], qk_gain)
    key_rows = head_norm(projected[:, head_width : 2 * head_width], qk_gain).reshape(
        row_count, head_width
    )
    value_rows = projected[:, 2 * head_width :].astype(jnp.bfloat16)
    score_scale = 1.0 / math.sqrt(HD)
    packed = jnp.concatenate([key_rows, value_rows], axis=1)
    gathered = lax.all_gather(packed, "tensor", axis=0, tiled=False)
    vocab_pack = jnp.concatenate(
        [w_vocab, logit_gain[None], jnp.zeros((7, w_vocab.shape[1]), w_vocab.dtype)], axis=0
    )
    vocab_pack, gathered = lax.optimization_barrier((vocab_pack, gathered))
    vocab_all = lax.all_gather(vocab_pack, "dp", axis=0, tiled=False)
    key_all = gathered[:, :row_count, :head_width].reshape(-1, head_width)
    value_all = gathered[:, :row_count, head_width:].reshape(-1, head_width)
    seg_all = lax.all_gather(segments, "tensor", axis=0, tiled=True)
    tally = jnp.sum((seg_all[:, None] == request_numbers[None, :]).astype(jnp.int32), axis=0)
    total_keys = key_all.shape[0]
    key_pos = jnp.arange(total_keys, dtype=jnp.int32)
    head_of_column = jnp.arange(head_width, dtype=jnp.int32) // HD
    head_mask = (jnp.arange(HEADS, dtype=jnp.int32)[:, None] == head_of_column[None, :]).astype(
        jnp.bfloat16
    )
    query_flat = queries.reshape(row_count, head_width)
    query_blocks = (query_flat[None, :, :] * head_mask[:, None, :]).reshape(
        HEADS * row_count, head_width
    )
    scores = (
        lax.dot_general(
            query_blocks,
            key_all,
            (((1,), (1,)), ((), ())),
            preferred_element_type=jnp.float32,
        ).reshape(HEADS, row_count, total_keys)
        * score_scale
    )
    allowed = (seg_all[None, :] == segments[:, None]) & (key_pos[None, :] <= positions[:, None])
    row_max = jnp.max(jnp.where(allowed[None], scores, NEGATIVE), axis=2)
    weights = jnp.where(allowed[None], jnp.exp(scores - row_max[:, :, None]), 0.0)
    weight_sum = jnp.sum(weights, axis=2)
    weighted = jnp.dot(
        weights.astype(jnp.bfloat16).reshape(HEADS * row_count, total_keys),
        value_all,
        preferred_element_type=jnp.float32,
    ).reshape(HEADS, row_count, head_width)
    attended = jnp.sum(
        (weighted / weight_sum[:, :, None]) * head_mask[:, None, :].astype(jnp.float32), axis=0
    ).astype(jnp.bfloat16)
    attn_rows = normalize(jnp.dot(attended, w_out, preferred_element_type=jnp.float32))
    residual_in = start_rows.astype(jnp.float32)
    mid_rows = normalize(residual_in + alpha_attn * (attn_rows - residual_in)).astype(jnp.bfloat16)
    mid_rows, vocab_all = lax.optimization_barrier((mid_rows, vocab_all))
    received = lax.all_gather(mid_rows, "dp", axis=0, tiled=True)
    up_proj = jnp.dot(received, w_up, preferred_element_type=jnp.float32) * up_gain
    gate_proj = jnp.dot(received, w_gate, preferred_element_type=jnp.float32) * gate_gain
    hidden = (up_proj * jax.nn.silu(gate_proj)).astype(jnp.bfloat16)
    mixed_sum = lax.psum_scatter(
        jnp.dot(hidden, w_down, preferred_element_type=jnp.float32).astype(jnp.bfloat16),
        "dp",
        scatter_dimension=0,
        tiled=True,
    ).astype(jnp.float32)
    mlp_rows = normalize(mixed_sum)
    residual_mid = mid_rows.astype(jnp.float32)
    result_rows = normalize(residual_mid + alpha_mlp * (mlp_rows - residual_mid)).astype(
        jnp.bfloat16
    )
    request_ends = jnp.cumsum(tally) - 1
    same_request = segments[:, None] == request_numbers[None, :]
    row_end = jnp.sum(jnp.where(same_request, request_ends[None, :], 0), axis=1)
    is_last = positions == row_end
    member = same_request.astype(jnp.float32)
    chosen = member * is_last[:, None].astype(jnp.float32)
    result_f32 = result_rows.astype(jnp.float32)
    row_sums = jnp.dot(
        member.T.astype(jnp.bfloat16), result_rows, preferred_element_type=jnp.float32
    )
    last_rows = jnp.dot(
        chosen.T.astype(jnp.bfloat16), result_rows, preferred_element_type=jnp.float32
    )
    partial = jnp.concatenate([row_sums, last_rows], axis=0)
    summed = jnp.sum(
        lax.all_gather(partial.astype(jnp.bfloat16), "tensor", axis=0, tiled=False).astype(
            jnp.float32
        ),
        axis=0,
    )
    row_sums, last_rows = summed[:REQS], summed[REQS:]
    counts = tally.astype(jnp.float32)
    request_mean = row_sums / counts[:, None]
    group_norm = jnp.sqrt(jnp.mean(request_mean * request_mean, axis=1))
    slot_count = lax.axis_size("dp") * REQS
    dp_index = lax.axis_index("dp")
    model_width = last_rows.shape[1]
    pack_logits = jnp.einsum(
        "rd,gdc->rgc",
        last_rows.astype(jnp.bfloat16),
        vocab_all[:, :model_width],
        preferred_element_type=jnp.float32,
    ) * vocab_all[None, :, model_width].astype(jnp.float32)
    pack_max = jnp.max(pack_logits.reshape(REQS, -1), axis=1)
    own_slot = jnp.arange(slot_count, dtype=jnp.int32) // REQS == dp_index
    spread_max = jnp.where(own_slot, jnp.tile(pack_max, slot_count // REQS), NEGATIVE)
    spread_norm = jnp.where(own_slot, jnp.tile(group_norm, slot_count // REQS), NEGATIVE)
    every = lax.pmax(jnp.concatenate([spread_max, spread_norm]), ("dp", "tensor"))
    every_max, every_norm = every[:slot_count], every[slot_count:]
    placement = (pack_of_group[:, None] == jnp.arange(slot_count, dtype=jnp.int32)[None, :]).astype(
        jnp.float32
    )
    request_norm = jnp.dot(every_norm, placement, precision=lax.Precision.HIGHEST)
    max_logit = jnp.dot(every_max, placement, precision=lax.Precision.HIGHEST)
    return (result_rows[None], request_norm, max_logit)


def solution(mesh):
    return jax.shard_map(
        local,
        mesh=mesh,
        in_specs=(
            P("dp", "tensor", None),
            P("dp", "tensor"),
            P(),
            P(),
            P(),
            P(),
            P(),
            P(None, "dp"),
            P(None, "dp"),
            P("dp"),
            P("dp"),
            P("dp", None),
            P(),
            P(None, ("dp", "tensor")),
            P(("dp", "tensor")),
        ),
        out_specs=(P("dp", "tensor", None), P(), P()),
        check_vma=False,
    )
```
